256 devices in a mesh: exp: 64 (over z, y, core), det: 4 (over x).
Axes of the slice: x: 4, y: 4, z: 8, core: 2. Of those that a mesh axis runs over, the one named last changes fastest.
Arguments:
- images: bfloat16 [2048, 8, 128, 128], P('exp', 'det'), may hold values from 0.5 to 2
- det_ids: int32 [2048, 8], P('exp', 'det'), may hold values from 0 to 7, each once within a row
- flat: float32 [8, 128, 128], P('det'), may hold values from 0.25 to 1.75
- backgrounds: float32 [2048, 8], P('exp', 'det'), may hold values from -3 to 3
- taps: bfloat16 [2048, 2, 15], P('exp'), may hold values from 0.019897461 to 0.25
- partner_dev: int32 [2048, 2], P('exp'), may hold values from 0 to 63, all different within a row; in each aligned block of 32 rows (0 to 31, 32 to 63, ...) at most 2 rows name the same one
- partner_slot: int32 [2048, 2], P('exp'), may hold values from 0 to 31
- offsets: int32 [2048, 2, 2], P('exp'), may hold values from -40 to 40
- pair_valid: int32 [2048, 2, 8], P('exp', None, 'det'), may hold values 0 or 1
Outputs:
- grad_flat: float32 [8, 128, 128], P('det', 'exp')
- grad_bkg: float32 [2048, 8], P('exp', 'det')
The draws below stay inside these ranges and needn't reach their ends.
Inputs may be any that keep to these rules, and one draw needn't show every extreme that they name: `partner_dev`: among the 32 exposures of one device, no partner device is named by more than 2 of them, and each exposure names 2 different partner devices.
All inputs are finite; a program needn't handle non-finite values. No bound on the sum of `pair_valid` on one device may be relied on, other than what follows from the above.
Results may differ from the reference program's by a relative error of at most 0.0003.
Values may be sent and summed in bfloat16 or wider, within the bound.
No kernel may reach another device: no remote copies, remote signals or barrier semaphores. Data moves between devices by JAX's collectives and lax.ppermute only.
A program may use at most 128 MiB of HBM per device.

```python
import math
import jax
import jax.numpy as jnp
import numpy as np
from jax import lax

P_SIZE = 128
TAPS = 15
OFF = 40
NB = 2
EXP_DEV = 32
EXPOSURE_COUNT = 2048
DET = 8
CAP = 2
N_EXP = 64


def touch_ends(array, rng, low, high):
    index_at = [jax.random.randint(jax.random.fold_in(rng, axis), (), 0, length) for axis, length in enumerate(array.shape)]
    longest = array.shape.index(max(array.shape))
    next_to = index_at[:longest] + [(index_at[longest] + 1) % array.shape[longest]] + index_at[longest + 1:]
    return array.at[tuple(index_at)].set(low).at[tuple(next_to)].set(high)


def levels(key, shape, pieces, least, largest):
    level = 1.0
    for dim, shards_of in pieces:
        steps = jax.random.uniform(jax.random.fold_in(jax.random.fold_in(key, 6), dim), (shards_of,), jnp.float32, least / len(pieces), largest / len(pieces))
        level = level * jnp.repeat(jnp.exp(steps), shape[dim] // shards_of).reshape((-1,) + (1,) * (len(shape) - 1 - dim))
    return level


def routed_block(own_key, own, number, rows, amount, top, limit, skew):
    order = jax.random.permutation(own_key, amount)
    heavy_load, usual = shares(amount, rows * top, limit, skew, True), shares(amount, rows * top, limit, skew, False)
    places = jnp.arange(amount)

    def named(lengths, turn):
        used = int((lengths > 0).sum())
        fixed = max(1, used // 4)
        moved = fixed + (places - fixed + turn * (used - fixed)) % max(1, amount - fixed)
        return jnp.zeros((amount,), jnp.int32).at[order[jnp.where(places < fixed, places, moved)]].set(jnp.asarray(lengths, jnp.int32))

    lengths = jnp.where(number % 4 == 0, named(heavy_load, number // 4), named(usual, number - number // 4 - 1))
    mixed = jax.random.permutation(jax.random.fold_in(own, 3), amount)
    giver, taker = mixed[0:amount // 2 * 2:2], mixed[1:amount // 2 * 2:2]
    room = jnp.minimum(lengths[giver] - 1, limit - lengths[taker]) // 2
    room = jnp.where((giver == order[0]) | (taker == order[0]) | (lengths[taker] == 0), 0, jnp.maximum(room, 0))
    moved = jax.random.randint(jax.random.fold_in(own, 4), (amount // 2,), 0, 1 << 20) % (room + 1)
    lengths = lengths.at[giver].add(-moved).at[taker].add(moved)
    labels = jnp.searchsorted(jnp.cumsum(lengths), jnp.arange(rows * top), side="right").astype(jnp.int32)
    listing = labels.reshape(top, rows).T
    listing = listing[jax.random.permutation(jax.random.fold_in(own, 1), rows)]
    turn = jax.random.randint(jax.random.fold_in(own, 2), (rows, 1), 0, top)
    return jnp.take_along_axis(listing, (jnp.arange(top)[None, :] + turn) % top, axis=1)


def shares(amount, total, reach, skew, full):
    weights = [(1 << 20) // math.isqrt(standing ** skew) + 1 for standing in range(1, amount + 1)]
    largest = reach if full else min(reach, max(-(-total // amount), total * weights[0] // sum(weights)))
    least = 1 if total - largest >= amount - 1 else 0
    counts, surplus = [largest] + [least] * (amount - 1), total - largest - least * (amount - 1)
    while surplus > 0:
        candidates = [i for i in range(1, amount) if counts[i] < largest] or [i for i in range(1, amount) if counts[i] < reach]
        pool, remaining = sum([weights[i] for i in candidates]), surplus
        for i in candidates:
            addition = min(reach - counts[i], max(1, remaining * weights[i] // pool), surplus)
            counts[i] = counts[i] + addition
            surplus = surplus - addition
    return np.array(counts)


def normal_values(rng, extent, spread, reach, pieces=(), kind=jnp.bfloat16):
    factor_of = levels(rng, extent, pieces, -0.22, 0.18) if pieces else 1.0
    drawn = jax.random.normal(rng, extent, jnp.float32) * spread * factor_of
    return jnp.minimum(jnp.maximum(drawn, -reach), reach).astype(kind)


def setup_inputs(seed: int = 0) -> dict:
    keys = jax.random.split(jax.random.key(seed), 10)
    images = jnp.clip(0.5 + 1.5 * jax.random.uniform(keys[0], (EXPOSURE_COUNT, DET, P_SIZE, P_SIZE), jnp.float32) ** levels(keys[0], (EXPOSURE_COUNT, DET, P_SIZE, P_SIZE), ((0, 64), (1, 4)), -0.2, 0.2), 0.5, 2.0).astype(jnp.bfloat16)
    det_ids = jax.vmap(lambda own: jax.random.permutation(own, DET))(jax.random.split(keys[1], EXPOSURE_COUNT)).reshape((EXPOSURE_COUNT, DET)).astype(jnp.int32)
    flat = jnp.clip(1.0 + 0.15 * jax.random.normal(keys[2], (DET, P_SIZE, P_SIZE), jnp.float32), 0.25, 1.75)
    backgrounds = normal_values(keys[3], (EXPOSURE_COUNT, DET), 0.5, 3.0, ((0, 64), (1, 4)), jnp.float32)
    taps = jnp.clip(jnp.exp(math.log(0.25) - 2.5308688 * jax.random.uniform(keys[4], (EXPOSURE_COUNT, 2, TAPS), jnp.float32) ** levels(keys[4], (EXPOSURE_COUNT, 2, TAPS), ((0, 64),), -0.2, 0.2)), 0.019897461, 0.25).astype(jnp.bfloat16)
    partner_dev_keys = jax.random.split(jax.random.fold_in(keys[5], 1), EXPOSURE_COUNT // EXP_DEV)
    partner_dev_turns = jax.random.permutation(jax.random.fold_in(keys[5], 3), EXPOSURE_COUNT // EXP_DEV)
    partner_dev = jax.vmap(lambda own, number: routed_block(jax.random.fold_in(keys[5], 2), own, number, EXP_DEV, N_EXP, NB, CAP, 2))(partner_dev_keys, partner_dev_turns).reshape((EXPOSURE_COUNT, NB))
    partner_slot = touch_ends(jax.random.randint(keys[6], (EXPOSURE_COUNT, NB), 0, EXP_DEV), jax.random.fold_in(keys[6], 1), 0, EXP_DEV - 1).astype(jnp.int32)
    offsets = touch_ends(jax.random.randint(keys[7], (EXPOSURE_COUNT, NB, 2), 0 - OFF, OFF + 1), jax.random.fold_in(keys[7], 1), 0 - OFF, OFF).astype(jnp.int32)
    pair_valid = touch_ends((jax.random.randint(keys[8], (EXPOSURE_COUNT, NB, DET), 0, 4) < 3).astype(jnp.int32), jax.random.fold_in(keys[8], 1), 0, 1)
    return {"images": images, "det_ids": det_ids, "flat": flat, "backgrounds": backgrounds, "taps": taps, "partner_dev": partner_dev, "partner_slot": partner_slot, "offsets": offsets, "pair_valid": pair_valid}


def band_matrices(taps):
    rows = jnp.arange(P_SIZE, dtype=jnp.int32)
    lag = rows[None, :] - rows[:, None] + (TAPS - 1) // 2
    inside = (lag >= 0) & (lag < TAPS)
    picked = jnp.take(taps, jnp.clip(lag, 0, TAPS - 1), axis=-1)
    return jnp.where(inside, picked, jnp.zeros_like(picked))

def shift_field(field, row_off, col_off):
    widths = [(0, 0)] * (field.ndim - 2) + [(OFF, OFF), (OFF, OFF)]
    padded = jnp.pad(field, widths)
    starts = [jnp.int32(0)] * (field.ndim - 2) + [(OFF + row_off).astype(jnp.int32), (OFF + col_off).astype(jnp.int32)]
    return lax.dynamic_slice(padded, starts, field.shape)

def intersection_mask(row_off, col_off):
    rows = jnp.arange(P_SIZE, dtype=jnp.int32)
    row_in = (rows + row_off >= 0) & (rows + row_off < P_SIZE)
    col_in = (rows + col_off >= 0) & (rows + col_off < P_SIZE)
    return (row_in[:, None] & col_in[None, :]).astype(jnp.float32)

def reference(images, det_ids, flat, backgrounds, taps, partner_dev, partner_slot, offsets, pair_valid):
    high = lax.Precision.HIGHEST
    bands = jax.vmap(band_matrices)(taps)

    def match_one(item):
        image, ids, background, band = item
        gain = flat[ids]
        calibrated = (gain * image.astype(jnp.float32) - background[:, None, None]).astype(jnp.bfloat16)
        kv = band[0].astype(jnp.float32)
        kh = band[1].astype(jnp.float32)
        half_done = jnp.einsum('dyw,xw->dyx', calibrated.astype(jnp.float32), kh, precision=high).astype(jnp.bfloat16)
        return jnp.einsum('vy,dyx->dvx', kv, half_done.astype(jnp.float32), precision=high).astype(jnp.bfloat16)
    psf_matched_images = lax.map(match_one, (images, det_ids, backgrounds, bands))
    partner_exposure = (partner_dev * EXP_DEV + partner_slot).reshape(-1).astype(jnp.int32)
    owner = jnp.repeat(jnp.arange(EXPOSURE_COUNT, dtype=jnp.int32), NB)
    shifts = offsets.reshape(-1, 2)
    weights = pair_valid.reshape(-1, DET).astype(jnp.float32)

    def pair_step(adjoint, item):
        own, other, shift, weight = item
        row_off = shift[0]
        col_off = shift[1]
        mine = psf_matched_images[own].astype(jnp.float32)
        theirs = psf_matched_images[other].astype(jnp.float32)
        resid = weight[:, None, None] * intersection_mask(row_off, col_off)[None] * (mine - shift_field(theirs, row_off, col_off))
        returned_images = lax.optimization_barrier(shift_field(resid, -row_off, -col_off).astype(jnp.bfloat16)).astype(jnp.float32)
        adjoint = adjoint.at[own].add(resid)
        adjoint = adjoint.at[other].add(-returned_images)
        return (adjoint, None)
    adjoint, _ = lax.scan(pair_step, jnp.zeros((EXPOSURE_COUNT, DET, P_SIZE, P_SIZE), jnp.float32), (owner, partner_exposure, shifts, weights))
    flat_norm = 1.0 / math.sqrt(2.0 * NB * EXPOSURE_COUNT)

    def finish(total, item):
        adj, image, ids, band = item
        kv = band[0].astype(jnp.float32)
        kh = band[1].astype(jnp.float32)
        partial_rows = jnp.einsum('dyx,xw->dyw', adj, kh, precision=high)
        adj_cal = jnp.einsum('yv,dyw->dvw', kv, partial_rows, precision=high)
        background_grad = -lax.optimization_barrier(jnp.sum(adj_cal, axis=(1, 2))) / P_SIZE
        pick = (ids[:, None] == jnp.arange(DET, dtype=jnp.int32)[None, :]).astype(jnp.float32)
        total = total + jnp.einsum('dg,dpq->gpq', pick, image.astype(jnp.float32) * adj_cal * flat_norm, precision=high)
        return (total, background_grad)
    grad_flat, grad_bkg = lax.scan(finish, jnp.zeros((DET, P_SIZE, P_SIZE), jnp.float32), (adjoint, images, det_ids, bands))
    return (grad_flat, grad_bkg)
```

```python
import math

import jax
import jax.numpy as jnp
from jax import lax
from jax.sharding import PartitionSpec as P


def shift_mats(offs, pixels):
    rows = jnp.arange(pixels, dtype=jnp.int32)
    return (rows[None, None, :] == rows[None, :, None] + offs[:, None, None]).astype(jnp.bfloat16)


def apply_shift(field, row_mats, col_mats):
    partial_cols = jnp.einsum(
        "qduv,qxv->qdux", field, col_mats, preferred_element_type=jnp.float32
    ).astype(jnp.bfloat16)
    return jnp.einsum("qyu,qdux->qdyx", row_mats, partial_cols, preferred_element_type=jnp.float32)


def intersection_masks(row_offs, col_offs, pixels):
    rows = jnp.arange(pixels, dtype=jnp.int32)
    row_in = (rows[None, :] + row_offs[:, None] >= 0) & (rows[None, :] + row_offs[:, None] < pixels)
    col_in = (rows[None, :] + col_offs[:, None] >= 0) & (rows[None, :] + col_offs[:, None] < pixels)
    return (row_in[:, :, None] & col_in[:, None, :]).astype(jnp.float32)


def body(images, det_ids, flat, backgrounds, taps, partner_dev, partner_slot, offsets, pair_valid):
    high = lax.Precision.HIGHEST
    exp_dev, det_dev, pixels = (images.shape[0], images.shape[1], images.shape[2])
    pair_count = partner_dev.shape[1]
    tap_count = taps.shape[2]
    n_exp = lax.axis_size("exp")
    exp_here = lax.axis_index("exp")
    det_here = lax.axis_index("det")
    queries = exp_dev * pair_count
    all_flat = lax.all_gather(flat, "det", axis=0, tiled=True)
    det_total = all_flat.shape[0]
    pick = (det_ids[:, :, None] == jnp.arange(det_total, dtype=jnp.int32)[None, None, :]).astype(
        jnp.float32
    )
    gains = jnp.einsum("edg,gpq->edpq", pick, all_flat, precision=high)
    calibrated = (gains * images.astype(jnp.float32) - backgrounds[:, :, None, None]).astype(
        jnp.bfloat16
    )
    rows = jnp.arange(pixels, dtype=jnp.int32)
    lag = rows[None, :] - rows[:, None] + (tap_count - 1) // 2
    table = (lag[:, :, None] == jnp.arange(tap_count, dtype=jnp.int32)[None, None, :]).astype(
        jnp.bfloat16
    )
    bands = jnp.einsum("pqt,ekt->ekpq", table, taps, preferred_element_type=jnp.float32).astype(
        jnp.bfloat16
    )
    along_rows = bands[:, 0]
    along_cols = bands[:, 1]
    half_done = jnp.einsum(
        "edyw,exw->edyx", calibrated, along_cols, preferred_element_type=jnp.float32
    ).astype(jnp.bfloat16)
    psf_matched_images = jnp.einsum(
        "evy,edyx->edvx", along_rows, half_done, preferred_element_type=jnp.float32
    ).astype(jnp.bfloat16)
    dest = partner_dev.reshape(-1)
    wanted = partner_slot.reshape(-1)
    row_offs = offsets[:, :, 0].reshape(-1)
    col_offs = offsets[:, :, 1].reshape(-1)
    valid_flat = pair_valid.reshape(queries, det_dev)
    cap = max(2, 2 * exp_dev * pair_count // n_exp)
    slots_all = n_exp * cap
    hits = (dest[:, None] == jnp.arange(n_exp, dtype=jnp.int32)[None, :]).astype(jnp.int32)
    before = jnp.cumsum(hits, axis=0) - hits
    rank = jnp.sum(before * hits, axis=1)
    slot = dest * cap + rank
    placement_table = (slot[None, :] == jnp.arange(slots_all, dtype=jnp.int32)[:, None]).astype(
        jnp.bfloat16
    )
    out_ids = jnp.zeros((slots_all,), jnp.int32).at[slot].set(wanted + 1).reshape(n_exp, cap)
    outgoing_shift = (
        jnp.zeros((slots_all, 2), jnp.int32)
        .at[slot]
        .set(offsets.reshape(queries, 2))
        .reshape(n_exp, cap, 2)
    )
    out_valid = (
        jnp.zeros((slots_all, det_dev), jnp.int32)
        .at[slot]
        .set(valid_flat)
        .reshape(n_exp, cap, det_dev)
    )
    in_ids, in_shift, in_valid = (
        lax.all_to_all(out_ids, "exp", split_axis=0, concat_axis=0, tiled=True),
        lax.all_to_all(outgoing_shift, "exp", split_axis=0, concat_axis=0, tiled=True),
        lax.all_to_all(out_valid, "exp", split_axis=0, concat_axis=0, tiled=True),
    )
    incoming = in_ids.reshape(-1)
    in_shift = in_shift.reshape(slots_all, 2)
    in_valid = in_valid.reshape(slots_all, det_dev)
    served_selection = (
        incoming[:, None] - 1 == jnp.arange(exp_dev, dtype=jnp.int32)[None, :]
    ).astype(jnp.bfloat16)
    served_flat = jnp.einsum(
        "lm,muqo->luqo", served_selection, psf_matched_images, preferred_element_type=jnp.float32
    ).astype(jnp.bfloat16)
    served = served_flat.reshape(n_exp, cap, det_dev, pixels, pixels)
    returned = lax.all_to_all(served, "exp", split_axis=0, concat_axis=0, tiled=True)
    partners = jnp.einsum(
        "fj,fvhm->jvhm",
        placement_table,
        returned.reshape(slots_all, det_dev, pixels, pixels),
        preferred_element_type=jnp.float32,
    ).astype(jnp.bfloat16)
    moved = apply_shift(partners, shift_mats(row_offs, pixels), shift_mats(col_offs, pixels))
    intersection = intersection_masks(row_offs, col_offs, pixels).reshape(
        exp_dev, pair_count, 1, pixels, pixels
    )
    weight = pair_valid.astype(jnp.float32).reshape(exp_dev, pair_count, det_dev, 1, 1)
    moved = moved.reshape(exp_dev, pair_count, det_dev, pixels, pixels)
    resid = weight * intersection * (psf_matched_images[:, None].astype(jnp.float32) - moved)
    adj_own = jnp.sum(resid, axis=1)
    resid_low = resid.reshape(queries, det_dev, pixels, pixels).astype(jnp.bfloat16)
    returned_images = apply_shift(
        resid_low, shift_mats(-row_offs, pixels), shift_mats(-col_offs, pixels)
    ).astype(jnp.bfloat16)
    sending_images = jnp.einsum(
        "ea,ajhv->ejhv", placement_table, returned_images, preferred_element_type=jnp.float32
    ).astype(jnp.bfloat16)
    sending_images = sending_images.reshape(n_exp, cap, det_dev, pixels, pixels)
    arrived = lax.all_to_all(
        sending_images, "exp", split_axis=0, concat_axis=0, tiled=True
    ).reshape(slots_all, det_dev, pixels, pixels)
    owners = (incoming[None, :] - 1 == jnp.arange(exp_dev, dtype=jnp.int32)[:, None]).astype(
        jnp.bfloat16
    )
    adj_partner = jnp.einsum("js,sdpq->jdpq", owners, arrived, preferred_element_type=jnp.float32)
    adj_matched = adj_own - adj_partner
    partial_rows = jnp.einsum(
        "edyx,exw->edyw", adj_matched, along_cols.astype(jnp.float32), precision=high
    )
    adj_cal = jnp.einsum(
        "eyv,edyw->edvw", along_rows.astype(jnp.float32), partial_rows, precision=high
    )
    grad_bkg = -jnp.sum(adj_cal, axis=(2, 3)) / pixels
    flat_norm = 1.0 / math.sqrt(2.0 * pair_count * exp_dev * n_exp)
    terms = jnp.einsum(
        "edg,edpq->gpq", pick, images.astype(jnp.float32) * adj_cal * flat_norm, precision=high
    )
    by_det = lax.psum_scatter(terms, "det", scatter_dimension=0, tiled=True)
    band_rows = pixels // n_exp
    by_band = by_det.reshape(det_dev, n_exp, band_rows, pixels).transpose(1, 0, 2, 3)
    grad_flat = jnp.sum(
        lax.all_to_all(by_band, "exp", split_axis=0, concat_axis=0, tiled=True), axis=0
    )
    return (grad_flat, grad_bkg)


def solution(mesh):
    return jax.shard_map(
        body,
        mesh=mesh,
        in_specs=(
            P("exp", "det", None, None),
            P("exp", "det"),
            P("det", None, None),
            P("exp", "det"),
            P("exp", None, None),
            P("exp", None),
            P("exp", None),
            P("exp", None, None),
            P("exp", None, "det"),
        ),
        out_specs=(P("det", "exp", None), P("exp", "det")),
        check_vma=False,
    )
```

```python
import math

import jax
import jax.numpy as jnp
from jax import lax
from jax.sharding import PartitionSpec as P


def shift_mats(offs, pixels):
    rows = jnp.arange(pixels, dtype=jnp.int32)
    return (rows[None, None, :] == rows[None, :, None] + offs[:, None, None]).astype(jnp.bfloat16)


def apply_shift(field, row_mats, col_mats):
    partial_cols = jnp.einsum(
        "qduv,qxv->qdux", field, col_mats, preferred_element_type=jnp.float32
    ).astype(jnp.bfloat16)
    return jnp.einsum("qyu,qdux->qdyx", row_mats, partial_cols, preferred_element_type=jnp.float32)


def intersection_masks(row_offs, col_offs, pixels):
    rows = jnp.arange(pixels, dtype=jnp.int32)
    row_in = (rows[None, :] + row_offs[:, None] >= 0) & (rows[None, :] + row_offs[:, None] < pixels)
    col_in = (rows[None, :] + col_offs[:, None] >= 0) & (rows[None, :] + col_offs[:, None] < pixels)
    return (row_in[:, :, None] & col_in[:, None, :]).astype(jnp.float32)


def body(images, det_ids, flat, backgrounds, taps, partner_dev, partner_slot, offsets, pair_valid):
    high = lax.Precision.HIGHEST
    exp_dev, det_dev, pixels = (images.shape[0], images.shape[1], images.shape[2])
    pair_count = partner_dev.shape[1]
    tap_count = taps.shape[2]
    n_exp = lax.axis_size("exp")
    queries = exp_dev * pair_count
    all_flat = lax.all_gather(flat, "det", axis=0, tiled=True)
    det_total = all_flat.shape[0]
    pick = (det_ids[:, :, None] == jnp.arange(det_total, dtype=jnp.int32)[None, None, :]).astype(
        jnp.float32
    )
    rows = jnp.arange(pixels, dtype=jnp.int32)
    lag = rows[None, :] - rows[:, None] + (tap_count - 1) // 2
    table = (lag[:, :, None] == jnp.arange(tap_count, dtype=jnp.int32)[None, None, :]).astype(
        jnp.bfloat16
    )
    bands = jnp.einsum("pqt,ekt->ekpq", table, taps, preferred_element_type=jnp.float32).astype(
        jnp.bfloat16
    )
    along_rows = bands[:, 0]
    along_cols = bands[:, 1]
    dest = partner_dev.reshape(-1)
    wanted = partner_slot.reshape(-1)
    row_offs = offsets[:, :, 0].reshape(-1)
    col_offs = offsets[:, :, 1].reshape(-1)
    valid_flat = pair_valid.reshape(queries, det_dev)
    cap = max(2, 2 * exp_dev * pair_count // n_exp)
    slots_all = n_exp * cap
    hits = (dest[:, None] == jnp.arange(n_exp, dtype=jnp.int32)[None, :]).astype(jnp.int32)
    before = jnp.cumsum(hits, axis=0) - hits
    rank = jnp.sum(before * hits, axis=1)
    slot = dest * cap + rank
    placement_table = (slot[None, :] == jnp.arange(slots_all, dtype=jnp.int32)[:, None]).astype(
        jnp.bfloat16
    )
    out_ids = jnp.zeros((slots_all,), jnp.int32).at[slot].set(wanted + 1).reshape(n_exp, cap)
    in_ids = lax.all_to_all(out_ids, "exp", split_axis=0, concat_axis=0, tiled=True)
    incoming = in_ids.reshape(-1)
    served_selection = (
        incoming[:, None] - 1 == jnp.arange(exp_dev, dtype=jnp.int32)[None, :]
    ).astype(jnp.bfloat16)
    owners = (incoming[None, :] - 1 == jnp.arange(exp_dev, dtype=jnp.int32)[:, None]).astype(
        jnp.bfloat16
    )
    fwd_rows = shift_mats(row_offs, pixels)
    fwd_cols = shift_mats(col_offs, pixels)
    back_rows = shift_mats(-row_offs, pixels)
    back_cols = shift_mats(-col_offs, pixels)
    intersection = intersection_masks(row_offs, col_offs, pixels).reshape(
        exp_dev, pair_count, 1, pixels, pixels
    )
    kv32 = along_rows.astype(jnp.float32)
    kh32 = along_cols.astype(jnp.float32)
    flat_norm = 1.0 / math.sqrt(2.0 * pair_count * exp_dev * n_exp)
    bkg_parts = []
    terms = None
    for dd in range(det_dev):
        sl = slice(dd, dd + 1)
        image_d = images[:, sl]
        pick_d = pick[:, sl]
        gains = jnp.einsum("edg,gpq->edpq", pick_d, all_flat, precision=high)
        calibrated = (gains * image_d.astype(jnp.float32) - backgrounds[:, sl, None, None]).astype(
            jnp.bfloat16
        )
        half_done = jnp.einsum(
            "edyw,exw->edyx", calibrated, along_cols, preferred_element_type=jnp.float32
        ).astype(jnp.bfloat16)
        matched = jnp.einsum(
            "evy,edyx->edvx", along_rows, half_done, preferred_element_type=jnp.float32
        ).astype(jnp.bfloat16)
        served = jnp.einsum(
            "lm,muqo->luqo", served_selection, matched, preferred_element_type=jnp.float32
        ).astype(jnp.bfloat16)
        served = served.reshape(n_exp, cap, 1, pixels, pixels)
        returned = lax.all_to_all(served, "exp", split_axis=0, concat_axis=0, tiled=True)
        partners = jnp.einsum(
            "fj,fvhm->jvhm",
            placement_table,
            returned.reshape(slots_all, 1, pixels, pixels),
            preferred_element_type=jnp.float32,
        ).astype(jnp.bfloat16)
        moved = apply_shift(partners, fwd_rows, fwd_cols)
        weight = valid_flat[:, sl].astype(jnp.float32).reshape(exp_dev, pair_count, 1, 1, 1)
        moved = moved.reshape(exp_dev, pair_count, 1, pixels, pixels)
        resid = weight * intersection * (matched[:, None].astype(jnp.float32) - moved)
        adj_own = jnp.sum(resid, axis=1)
        resid_low = resid.reshape(queries, 1, pixels, pixels).astype(jnp.bfloat16)
        returned_images = apply_shift(resid_low, back_rows, back_cols).astype(jnp.bfloat16)
        sending_images = jnp.einsum(
            "ea,ajhv->ejhv", placement_table, returned_images, preferred_element_type=jnp.float32
        ).astype(jnp.bfloat16)
        sending_images = sending_images.reshape(n_exp, cap, 1, pixels, pixels)
        arrived = lax.all_to_all(
            sending_images, "exp", split_axis=0, concat_axis=0, tiled=True
        ).reshape(slots_all, 1, pixels, pixels)
        adj_partner = jnp.einsum(
            "js,sdpq->jdpq", owners, arrived, preferred_element_type=jnp.float32
        )
        adj_matched = adj_own - adj_partner
        partial_rows = jnp.einsum("edyx,exw->edyw", adj_matched, kh32, precision=high)
        adj_cal = jnp.einsum("eyv,edyw->edvw", kv32, partial_rows, precision=high)
        bkg_parts.append(-jnp.sum(adj_cal, axis=(2, 3)) / pixels)
        part = jnp.einsum(
            "edg,edpq->gpq", pick_d, image_d.astype(jnp.float32) * adj_cal * flat_norm,
            precision=high,
        )
        terms = part if terms is None else terms + part
    grad_bkg = jnp.concatenate(bkg_parts, axis=1)
    band_rows = pixels // n_exp
    by_det = lax.psum_scatter(terms, "det", scatter_dimension=0, tiled=True)
    by_band = by_det.reshape(det_dev, n_exp, band_rows, pixels).transpose(1, 0, 2, 3)
    grad_flat = jnp.sum(
        lax.all_to_all(by_band, "exp", split_axis=0, concat_axis=0, tiled=True), axis=0
    )
    return (grad_flat, grad_bkg)


def solution(mesh):
    return jax.shard_map(
        body,
        mesh=mesh,
        in_specs=(
            P("exp", "det", None, None),
            P("exp", "det"),
            P("det", None, None),
            P("exp", "det"),
            P("exp", None, None),
            P("exp", None),
            P("exp", None),
            P("exp", None, None),
            P("exp", None, "det"),
        ),
        out_specs=(P("det", "exp", None), P("exp", "det")),
        check_vma=False,
    )
```

```python
import math

import jax
import jax.numpy as jnp
from jax import lax
from jax.sharding import PartitionSpec as P


def shift_mats(offs, pixels):
    rows = jnp.arange(pixels, dtype=jnp.int32)
    return (rows[None, None, :] == rows[None, :, None] + offs[:, None, None]).astype(jnp.bfloat16)


def apply_shift(field, row_mats, col_mats):
    partial_cols = jnp.einsum(
        "qduv,qxv->qdux", field, col_mats, preferred_element_type=jnp.float32
    ).astype(jnp.bfloat16)
    return jnp.einsum("qyu,qdux->qdyx", row_mats, partial_cols, preferred_element_type=jnp.float32)


def intersection_masks(row_offs, col_offs, pixels):
    rows = jnp.arange(pixels, dtype=jnp.int32)
    row_in = (rows[None, :] + row_offs[:, None] >= 0) & (rows[None, :] + row_offs[:, None] < pixels)
    col_in = (rows[None, :] + col_offs[:, None] >= 0) & (rows[None, :] + col_offs[:, None] < pixels)
    return (row_in[:, :, None] & col_in[:, None, :]).astype(jnp.float32)


def body(images, det_ids, flat, backgrounds, taps, partner_dev, partner_slot, offsets, pair_valid):
    high = lax.Precision.HIGHEST
    exp_dev, det_dev, pixels = (images.shape[0], images.shape[1], images.shape[2])
    pair_count = partner_dev.shape[1]
    tap_count = taps.shape[2]
    n_exp = lax.axis_size("exp")
    queries = exp_dev * pair_count
    all_flat = lax.all_gather(flat, "det", axis=0, tiled=True)
    det_total = all_flat.shape[0]
    pick = (det_ids[:, :, None] == jnp.arange(det_total, dtype=jnp.int32)[None, None, :]).astype(
        jnp.float32
    )
    rows = jnp.arange(pixels, dtype=jnp.int32)
    lag = rows[None, :] - rows[:, None] + (tap_count - 1) // 2
    table = (lag[:, :, None] == jnp.arange(tap_count, dtype=jnp.int32)[None, None, :]).astype(
        jnp.bfloat16
    )
    bands = jnp.einsum("pqt,ekt->ekpq", table, taps, preferred_element_type=jnp.float32).astype(
        jnp.bfloat16
    )
    along_rows = bands[:, 0]
    along_cols = bands[:, 1]
    dest = partner_dev.reshape(-1)
    wanted = partner_slot.reshape(-1)
    row_offs = offsets[:, :, 0].reshape(-1)
    col_offs = offsets[:, :, 1].reshape(-1)
    valid_flat = pair_valid.reshape(queries, det_dev)
    cap = max(2, 2 * exp_dev * pair_count // n_exp)
    slots_all = n_exp * cap
    hits = (dest[:, None] == jnp.arange(n_exp, dtype=jnp.int32)[None, :]).astype(jnp.int32)
    before = jnp.cumsum(hits, axis=0) - hits
    rank = jnp.sum(before * hits, axis=1)
    slot = dest * cap + rank
    placement_table = (slot[None, :] == jnp.arange(slots_all, dtype=jnp.int32)[:, None]).astype(
        jnp.bfloat16
    )
    out_ids = jnp.zeros((slots_all,), jnp.int32).at[slot].set(wanted + 1).reshape(n_exp, cap)
    in_ids = lax.all_to_all(out_ids, "exp", split_axis=0, concat_axis=0, tiled=True)
    incoming = in_ids.reshape(-1)
    served_selection = (
        incoming[:, None] - 1 == jnp.arange(exp_dev, dtype=jnp.int32)[None, :]
    ).astype(jnp.bfloat16)
    owners = (incoming[None, :] - 1 == jnp.arange(exp_dev, dtype=jnp.int32)[:, None]).astype(
        jnp.bfloat16
    )
    fwd_rows = shift_mats(row_offs, pixels)
    fwd_cols = shift_mats(col_offs, pixels)
    back_rows = shift_mats(-row_offs, pixels)
    back_cols = shift_mats(-col_offs, pixels)
    intersection = intersection_masks(row_offs, col_offs, pixels).reshape(
        exp_dev, pair_count, 1, pixels, pixels
    )
    kv32 = along_rows.astype(jnp.float32)
    kh32 = along_cols.astype(jnp.float32)
    flat_norm = 1.0 / math.sqrt(2.0 * pair_count * exp_dev * n_exp)
    bkg_parts = []
    terms = None
    for dd in range(det_dev):
        sl = slice(dd, dd + 1)
        image_d = images[:, sl]
        pick_d = pick[:, sl]
        gains = jnp.einsum("edg,gpq->edpq", pick_d, all_flat, precision=high)
        calibrated = (gains * image_d.astype(jnp.float32) - backgrounds[:, sl, None, None]).astype(
            jnp.bfloat16
        )
        half_done = jnp.einsum(
            "edyw,exw->edyx", calibrated, along_cols, preferred_element_type=jnp.float32
        ).astype(jnp.bfloat16)
        matched = jnp.einsum(
            "evy,edyx->edvx", along_rows, half_done, preferred_element_type=jnp.float32
        ).astype(jnp.bfloat16)
        served = jnp.einsum(
            "lm,muqo->luqo", served_selection, matched, preferred_element_type=jnp.float32
        ).astype(jnp.bfloat16)
        served = served.reshape(n_exp, cap * pixels, pixels)
        returned = lax.all_to_all(served, "exp", split_axis=0, concat_axis=0, tiled=True)
        partners = jnp.einsum(
            "fj,fvhm->jvhm",
            placement_table,
            returned.reshape(slots_all, 1, pixels, pixels),
            preferred_element_type=jnp.float32,
        ).astype(jnp.bfloat16)
        moved = apply_shift(partners, fwd_rows, fwd_cols)
        weight = valid_flat[:, sl].astype(jnp.float32).reshape(exp_dev, pair_count, 1, 1, 1)
        moved = moved.reshape(exp_dev, pair_count, 1, pixels, pixels)
        resid = weight * intersection * (matched[:, None].astype(jnp.float32) - moved)
        adj_own = jnp.sum(resid, axis=1)
        resid_low = resid.reshape(queries, 1, pixels, pixels).astype(jnp.bfloat16)
        returned_images = apply_shift(resid_low, back_rows, back_cols).astype(jnp.bfloat16)
        sending_images = jnp.einsum(
            "ea,ajhv->ejhv", placement_table, returned_images, preferred_element_type=jnp.float32
        ).astype(jnp.bfloat16)
        sending_images = sending_images.reshape(n_exp, cap * pixels, pixels)
        arrived = lax.all_to_all(
            sending_images, "exp", split_axis=0, concat_axis=0, tiled=True
        ).reshape(slots_all, 1, pixels, pixels)
        adj_partner = jnp.einsum(
            "js,sdpq->jdpq", owners, arrived, preferred_element_type=jnp.float32
        )
        adj_matched = adj_own - adj_partner
        partial_rows = jnp.einsum("edyx,exw->edyw", adj_matched, kh32, precision=high)
        adj_cal = jnp.einsum("eyv,edyw->edvw", kv32, partial_rows, precision=high)
        bkg_parts.append(-jnp.sum(adj_cal, axis=(2, 3)) / pixels)
        part = jnp.einsum(
            "edg,edpq->gpq", pick_d, image_d.astype(jnp.float32) * adj_cal * flat_norm,
            precision=high,
        )
        terms = part if terms is None else terms + part
    grad_bkg = jnp.concatenate(bkg_parts, axis=1)
    band_rows = pixels // n_exp
    by_det = lax.psum_scatter(terms, "det", scatter_dimension=0, tiled=True)
    by_band = by_det.reshape(det_dev, n_exp, band_rows, pixels).transpose(1, 0, 2, 3)
    grad_flat = jnp.sum(
        lax.all_to_all(by_band, "exp", split_axis=0, concat_axis=0, tiled=True), axis=0
    )
    return (grad_flat, grad_bkg)


def solution(mesh):
    return jax.shard_map(
        body,
        mesh=mesh,
        in_specs=(
            P("exp", "det", None, None),
            P("exp", "det"),
            P("det", None, None),
            P("exp", "det"),
            P("exp", None, None),
            P("exp", None),
            P("exp", None),
            P("exp", None, None),
            P("exp", None, "det"),
        ),
        out_specs=(P("det", "exp", None), P("exp", "det")),
        check_vma=False,
    )
```

```python
import math

import jax
import jax.numpy as jnp
from jax import lax
from jax.sharding import PartitionSpec as P


def shift_mats(offs, pixels):
    rows = jnp.arange(pixels, dtype=jnp.int32)
    return (rows[None, None, :] == rows[None, :, None] + offs[:, None, None]).astype(jnp.bfloat16)


def apply_shift(field, row_mats, col_mats):
    partial_cols = jnp.einsum(
        "qduv,qxv->qdux", field, col_mats, preferred_element_type=jnp.float32
    ).astype(jnp.bfloat16)
    return jnp.einsum("qyu,qdux->qdyx", row_mats, partial_cols, preferred_element_type=jnp.float32)


def intersection_masks(row_offs, col_offs, pixels):
    rows = jnp.arange(pixels, dtype=jnp.int32)
    row_in = (rows[None, :] + row_offs[:, None] >= 0) & (rows[None, :] + row_offs[:, None] < pixels)
    col_in = (rows[None, :] + col_offs[:, None] >= 0) & (rows[None, :] + col_offs[:, None] < pixels)
    return (row_in[:, :, None] & col_in[:, None, :]).astype(jnp.float32)


def body(images, det_ids, flat, backgrounds, taps, partner_dev, partner_slot, offsets, pair_valid):
    high = lax.Precision.HIGHEST
    exp_dev, det_dev, pixels = (images.shape[0], images.shape[1], images.shape[2])
    pair_count = partner_dev.shape[1]
    tap_count = taps.shape[2]
    n_exp = lax.axis_size("exp")
    exp_here = lax.axis_index("exp")
    det_here = lax.axis_index("det")
    queries = exp_dev * pair_count
    all_flat = lax.all_gather(flat, "det", axis=0, tiled=True)
    det_total = all_flat.shape[0]
    pick = (det_ids[:, :, None] == jnp.arange(det_total, dtype=jnp.int32)[None, None, :]).astype(
        jnp.float32
    )
    gains = jnp.einsum("edg,gpq->edpq", pick, all_flat, precision=high)
    calibrated = (gains * images.astype(jnp.float32) - backgrounds[:, :, None, None]).astype(
        jnp.bfloat16
    )
    rows = jnp.arange(pixels, dtype=jnp.int32)
    lag = rows[None, :] - rows[:, None] + (tap_count - 1) // 2
    table = (lag[:, :, None] == jnp.arange(tap_count, dtype=jnp.int32)[None, None, :]).astype(
        jnp.bfloat16
    )
    bands = jnp.einsum("pqt,ekt->ekpq", table, taps, preferred_element_type=jnp.float32).astype(
        jnp.bfloat16
    )
    along_rows = bands[:, 0]
    along_cols = bands[:, 1]
    half_done = jnp.einsum(
        "edyw,exw->edyx", calibrated, along_cols, preferred_element_type=jnp.float32
    ).astype(jnp.bfloat16)
    psf_matched_images = jnp.einsum(
        "evy,edyx->edvx", along_rows, half_done, preferred_element_type=jnp.float32
    ).astype(jnp.bfloat16)
    dest = partner_dev.reshape(-1)
    wanted = partner_slot.reshape(-1)
    row_offs = offsets[:, :, 0].reshape(-1)
    col_offs = offsets[:, :, 1].reshape(-1)
    valid_flat = pair_valid.reshape(queries, det_dev)
    cap = max(2, 2 * exp_dev * pair_count // n_exp)
    slots_all = n_exp * cap
    hits = (dest[:, None] == jnp.arange(n_exp, dtype=jnp.int32)[None, :]).astype(jnp.int32)
    before = jnp.cumsum(hits, axis=0) - hits
    rank = jnp.sum(before * hits, axis=1)
    slot = dest * cap + rank
    placement_table = (slot[None, :] == jnp.arange(slots_all, dtype=jnp.int32)[:, None]).astype(
        jnp.bfloat16
    )
    out_ids = jnp.zeros((slots_all,), jnp.int32).at[slot].set(wanted + 1).reshape(n_exp, cap)
    outgoing_shift = (
        jnp.zeros((slots_all, 2), jnp.int32)
        .at[slot]
        .set(offsets.reshape(queries, 2))
        .reshape(n_exp, cap, 2)
    )
    out_valid = (
        jnp.zeros((slots_all, det_dev), jnp.int32)
        .at[slot]
        .set(valid_flat)
        .reshape(n_exp, cap, det_dev)
    )
    in_ids, in_shift, in_valid = (
        lax.all_to_all(out_ids, "exp", split_axis=0, concat_axis=0, tiled=True),
        lax.all_to_all(outgoing_shift, "exp", split_axis=0, concat_axis=0, tiled=True),
        lax.all_to_all(out_valid, "exp", split_axis=0, concat_axis=0, tiled=True),
    )
    incoming = in_ids.reshape(-1)
    in_shift = in_shift.reshape(slots_all, 2)
    in_valid = in_valid.reshape(slots_all, det_dev)
    served_selection = (
        incoming[:, None] - 1 == jnp.arange(exp_dev, dtype=jnp.int32)[None, :]
    ).astype(jnp.bfloat16)
    served_flat = jnp.einsum(
        "lm,muqo->luqo", served_selection, psf_matched_images, preferred_element_type=jnp.float32
    ).astype(jnp.bfloat16)
    served = served_flat.reshape(n_exp, cap * det_dev * pixels, pixels)
    returned = lax.all_to_all(served, "exp", split_axis=0, concat_axis=0, tiled=True)
    partners = jnp.einsum(
        "fj,fvhm->jvhm",
        placement_table,
        returned.reshape(slots_all, det_dev, pixels, pixels),
        preferred_element_type=jnp.float32,
    ).astype(jnp.bfloat16)
    moved = apply_shift(partners, shift_mats(row_offs, pixels), shift_mats(col_offs, pixels))
    intersection = intersection_masks(row_offs, col_offs, pixels).reshape(
        exp_dev, pair_count, 1, pixels, pixels
    )
    weight = pair_valid.astype(jnp.float32).reshape(exp_dev, pair_count, det_dev, 1, 1)
    moved = moved.reshape(exp_dev, pair_count, det_dev, pixels, pixels)
    resid = weight * intersection * (psf_matched_images[:, None].astype(jnp.float32) - moved)
    adj_own = jnp.sum(resid, axis=1)
    resid_low = resid.reshape(queries, det_dev, pixels, pixels).astype(jnp.bfloat16)
    returned_images = apply_shift(
        resid_low, shift_mats(-row_offs, pixels), shift_mats(-col_offs, pixels)
    ).astype(jnp.bfloat16)
    sending_images = jnp.einsum(
        "ea,ajhv->ejhv", placement_table, returned_images, preferred_element_type=jnp.float32
    ).astype(jnp.bfloat16)
    sending_images = sending_images.reshape(n_exp, cap * det_dev * pixels, pixels)
    arrived = lax.all_to_all(
        sending_images, "exp", split_axis=0, concat_axis=0, tiled=True
    ).reshape(slots_all, det_dev, pixels, pixels)
    owners = (incoming[None, :] - 1 == jnp.arange(exp_dev, dtype=jnp.int32)[:, None]).astype(
        jnp.bfloat16
    )
    adj_partner = jnp.einsum("js,sdpq->jdpq", owners, arrived, preferred_element_type=jnp.float32)
    adj_matched = adj_own - adj_partner
    partial_rows = jnp.einsum(
        "edyx,exw->edyw", adj_matched, along_cols.astype(jnp.float32), precision=high
    )
    adj_cal = jnp.einsum(
        "eyv,edyw->edvw", along_rows.astype(jnp.float32), partial_rows, precision=high
    )
    grad_bkg = -jnp.sum(adj_cal, axis=(2, 3)) / pixels
    flat_norm = 1.0 / math.sqrt(2.0 * pair_count * exp_dev * n_exp)
    terms = jnp.einsum(
        "edg,edpq->gpq", pick, images.astype(jnp.float32) * adj_cal * flat_norm, precision=high
    )
    band_rows = pixels // n_exp
    n_det = det_total // det_dev
    by_block = (
        terms.reshape(n_det, det_dev, n_exp, band_rows, pixels)
        .transpose(2, 0, 1, 3, 4)
        .reshape(n_exp * n_det, det_dev, band_rows, pixels)
    )
    grad_flat = jnp.sum(
        lax.all_to_all(by_block, ("exp", "det"), split_axis=0, concat_axis=0, tiled=True),
        axis=0,
    )
    return (grad_flat, grad_bkg)


def solution(mesh):
    return jax.shard_map(
        body,
        mesh=mesh,
        in_specs=(
            P("exp", "det", None, None),
            P("exp", "det"),
            P("det", None, None),
            P("exp", "det"),
            P("exp", None, None),
            P("exp", None),
            P("exp", None),
            P("exp", None, None),
            P("exp", None, "det"),
        ),
        out_specs=(P("det", "exp", None), P("exp", "det")),
        check_vma=False,
    )
```

```python
import math

import jax
import jax.numpy as jnp
from jax import lax
from jax.sharding import PartitionSpec as P


def shift_mats(offs, pixels):
    rows = jnp.arange(pixels, dtype=jnp.int32)
    return (rows[None, None, :] == rows[None, :, None] + offs[:, None, None]).astype(jnp.bfloat16)


def apply_shift(field, row_mats, col_mats):
    partial_cols = jnp.einsum(
        "qduv,qxv->qdux", field, col_mats, preferred_element_type=jnp.float32
    ).astype(jnp.bfloat16)
    return jnp.einsum("qyu,qdux->qdyx", row_mats, partial_cols, preferred_element_type=jnp.float32)


def intersection_masks(row_offs, col_offs, pixels):
    rows = jnp.arange(pixels, dtype=jnp.int32)
    row_in = (rows[None, :] + row_offs[:, None] >= 0) & (rows[None, :] + row_offs[:, None] < pixels)
    col_in = (rows[None, :] + col_offs[:, None] >= 0) & (rows[None, :] + col_offs[:, None] < pixels)
    return (row_in[:, :, None] & col_in[:, None, :]).astype(jnp.float32)


def body(images, det_ids, flat, backgrounds, taps, partner_dev, partner_slot, offsets, pair_valid):
    high = lax.Precision.HIGHEST
    exp_dev, det_dev, pixels = (images.shape[0], images.shape[1], images.shape[2])
    pair_count = partner_dev.shape[1]
    tap_count = taps.shape[2]
    n_exp = lax.axis_size("exp")
    exp_here = lax.axis_index("exp")
    det_here = lax.axis_index("det")
    queries = exp_dev * pair_count
    all_flat = lax.all_gather(flat, "det", axis=0, tiled=True)
    det_total = all_flat.shape[0]
    pick = (det_ids[:, :, None] == jnp.arange(det_total, dtype=jnp.int32)[None, None, :]).astype(
        jnp.float32
    )
    gains = jnp.einsum("edg,gpq->edpq", pick, all_flat, precision=high)
    calibrated = (gains * images.astype(jnp.float32) - backgrounds[:, :, None, None]).astype(
        jnp.bfloat16
    )
    rows = jnp.arange(pixels, dtype=jnp.int32)
    lag = rows[None, :] - rows[:, None] + (tap_count - 1) // 2
    table = (lag[:, :, None] == jnp.arange(tap_count, dtype=jnp.int32)[None, None, :]).astype(
        jnp.bfloat16
    )
    bands = jnp.einsum("pqt,ekt->ekpq", table, taps, preferred_element_type=jnp.float32).astype(
        jnp.bfloat16
    )
    along_rows = bands[:, 0]
    along_cols = bands[:, 1]
    half_done = jnp.einsum(
        "edyw,exw->edyx", calibrated, along_cols, preferred_element_type=jnp.float32
    ).astype(jnp.bfloat16)
    psf_matched_images = jnp.einsum(
        "evy,edyx->edvx", along_rows, half_done, preferred_element_type=jnp.float32
    ).astype(jnp.bfloat16)
    dest = partner_dev.reshape(-1)
    wanted = partner_slot.reshape(-1)
    row_offs = offsets[:, :, 0].reshape(-1)
    col_offs = offsets[:, :, 1].reshape(-1)
    valid_flat = pair_valid.reshape(queries, det_dev)
    cap = max(2, 2 * exp_dev * pair_count // n_exp)
    slots_all = n_exp * cap
    hits = (dest[:, None] == jnp.arange(n_exp, dtype=jnp.int32)[None, :]).astype(jnp.int32)
    before = jnp.cumsum(hits, axis=0) - hits
    rank = jnp.sum(before * hits, axis=1)
    slot = dest * cap + rank
    placement_table = (slot[None, :] == jnp.arange(slots_all, dtype=jnp.int32)[:, None]).astype(
        jnp.bfloat16
    )
    out_ids = jnp.zeros((slots_all,), jnp.int32).at[slot].set(wanted + 1).reshape(n_exp, cap)
    outgoing_shift = (
        jnp.zeros((slots_all, 2), jnp.int32)
        .at[slot]
        .set(offsets.reshape(queries, 2))
        .reshape(n_exp, cap, 2)
    )
    out_valid = (
        jnp.zeros((slots_all, det_dev), jnp.int32)
        .at[slot]
        .set(valid_flat)
        .reshape(n_exp, cap, det_dev)
    )
    in_ids, in_shift, in_valid = (
        lax.all_to_all(out_ids, "exp", split_axis=0, concat_axis=0, tiled=True),
        lax.all_to_all(outgoing_shift, "exp", split_axis=0, concat_axis=0, tiled=True),
        lax.all_to_all(out_valid, "exp", split_axis=0, concat_axis=0, tiled=True),
    )
    incoming = in_ids.reshape(-1)
    in_shift = in_shift.reshape(slots_all, 2)
    in_valid = in_valid.reshape(slots_all, det_dev)
    served_selection = (
        incoming[:, None] - 1 == jnp.arange(exp_dev, dtype=jnp.int32)[None, :]
    ).astype(jnp.bfloat16)
    image_elems = det_dev * pixels * pixels
    served_flat = jnp.dot(
        served_selection,
        psf_matched_images.reshape(exp_dev, image_elems),
        preferred_element_type=jnp.float32,
    ).astype(jnp.bfloat16)
    served = served_flat.reshape(n_exp, cap * det_dev * pixels, pixels)
    returned = lax.all_to_all(served, "exp", split_axis=0, concat_axis=0, tiled=True)
    partners = (
        lax.dot_general(
            placement_table,
            returned.reshape(slots_all, image_elems),
            (((0,), (0,)), ((), ())),
            preferred_element_type=jnp.float32,
        )
        .astype(jnp.bfloat16)
        .reshape(queries, det_dev, pixels, pixels)
    )
    moved = apply_shift(partners, shift_mats(row_offs, pixels), shift_mats(col_offs, pixels))
    intersection = intersection_masks(row_offs, col_offs, pixels).reshape(
        exp_dev, pair_count, 1, pixels, pixels
    )
    weight = pair_valid.astype(jnp.float32).reshape(exp_dev, pair_count, det_dev, 1, 1)
    moved = moved.reshape(exp_dev, pair_count, det_dev, pixels, pixels)
    resid = weight * intersection * (psf_matched_images[:, None].astype(jnp.float32) - moved)
    adj_own = jnp.sum(resid, axis=1)
    resid_low = resid.reshape(queries, det_dev, pixels, pixels).astype(jnp.bfloat16)
    returned_images = apply_shift(
        resid_low, shift_mats(-row_offs, pixels), shift_mats(-col_offs, pixels)
    ).astype(jnp.bfloat16)
    sending_images = jnp.dot(
        placement_table,
        returned_images.reshape(queries, image_elems),
        preferred_element_type=jnp.float32,
    ).astype(jnp.bfloat16)
    sending_images = sending_images.reshape(n_exp, cap * det_dev * pixels, pixels)
    arrived = lax.all_to_all(
        sending_images, "exp", split_axis=0, concat_axis=0, tiled=True
    ).reshape(slots_all, image_elems)
    owners = (incoming[None, :] - 1 == jnp.arange(exp_dev, dtype=jnp.int32)[:, None]).astype(
        jnp.bfloat16
    )
    adj_partner = jnp.dot(owners, arrived, preferred_element_type=jnp.float32).reshape(
        exp_dev, det_dev, pixels, pixels
    )
    adj_matched = adj_own - adj_partner
    partial_rows = jnp.einsum(
        "edyx,exw->edyw", adj_matched, along_cols.astype(jnp.float32), precision=high
    )
    adj_cal = jnp.einsum(
        "eyv,edyw->edvw", along_rows.astype(jnp.float32), partial_rows, precision=high
    )
    grad_bkg = -jnp.sum(adj_cal, axis=(2, 3)) / pixels
    flat_norm = 1.0 / math.sqrt(2.0 * pair_count * exp_dev * n_exp)
    terms = jnp.einsum(
        "edg,edpq->gpq", pick, images.astype(jnp.float32) * adj_cal * flat_norm, precision=high
    )
    band_rows = pixels // n_exp
    n_det = det_total // det_dev
    by_block = (
        terms.reshape(n_det, det_dev, n_exp, band_rows, pixels)
        .transpose(2, 0, 1, 3, 4)
        .reshape(n_exp * n_det, det_dev, band_rows, pixels)
    )
    grad_flat = jnp.sum(
        lax.all_to_all(by_block, ("exp", "det"), split_axis=0, concat_axis=0, tiled=True),
        axis=0,
    )
    return (grad_flat, grad_bkg)


def solution(mesh):
    return jax.shard_map(
        body,
        mesh=mesh,
        in_specs=(
            P("exp", "det", None, None),
            P("exp", "det"),
            P("det", None, None),
            P("exp", "det"),
            P("exp", None, None),
            P("exp", None),
            P("exp", None),
            P("exp", None, None),
            P("exp", None, "det"),
        ),
        out_specs=(P("det", "exp", None), P("exp", "det")),
        check_vma=False,
    )
```

```python
import math

import jax
import jax.numpy as jnp
from jax import lax
from jax.sharding import PartitionSpec as P


def shift_mats(offs, pixels):
    rows = jnp.arange(pixels, dtype=jnp.int32)
    return (rows[None, None, :] == rows[None, :, None] + offs[:, None, None]).astype(jnp.bfloat16)


def apply_shift(field, row_mats, col_mats):
    partial_cols = jnp.einsum(
        "qduv,qxv->qdux", field, col_mats, preferred_element_type=jnp.float32
    ).astype(jnp.bfloat16)
    return jnp.einsum("qyu,qdux->qdyx", row_mats, partial_cols, preferred_element_type=jnp.float32)


def intersection_masks(row_offs, col_offs, pixels):
    rows = jnp.arange(pixels, dtype=jnp.int32)
    row_in = (rows[None, :] + row_offs[:, None] >= 0) & (rows[None, :] + row_offs[:, None] < pixels)
    col_in = (rows[None, :] + col_offs[:, None] >= 0) & (rows[None, :] + col_offs[:, None] < pixels)
    return (row_in[:, :, None] & col_in[:, None, :]).astype(jnp.float32)


def body(images, det_ids, flat, backgrounds, taps, partner_dev, partner_slot, offsets, pair_valid):
    high = lax.Precision.HIGHEST
    exp_dev, det_dev, pixels = (images.shape[0], images.shape[1], images.shape[2])
    pair_count = partner_dev.shape[1]
    tap_count = taps.shape[2]
    n_exp = lax.axis_size("exp")
    queries = exp_dev * pair_count
    all_flat = lax.all_gather(flat, "det", axis=0, tiled=True)
    det_total = all_flat.shape[0]
    pick = (det_ids[:, :, None] == jnp.arange(det_total, dtype=jnp.int32)[None, None, :]).astype(
        jnp.float32
    )
    rows = jnp.arange(pixels, dtype=jnp.int32)
    lag = rows[None, :] - rows[:, None] + (tap_count - 1) // 2
    table = (lag[:, :, None] == jnp.arange(tap_count, dtype=jnp.int32)[None, None, :]).astype(
        jnp.bfloat16
    )
    bands = jnp.einsum("pqt,ekt->ekpq", table, taps, preferred_element_type=jnp.float32).astype(
        jnp.bfloat16
    )
    along_rows = bands[:, 0]
    along_cols = bands[:, 1]
    dest = partner_dev.reshape(-1)
    wanted = partner_slot.reshape(-1)
    row_offs = offsets[:, :, 0].reshape(-1)
    col_offs = offsets[:, :, 1].reshape(-1)
    valid_flat = pair_valid.reshape(queries, det_dev)
    cap = max(2, 2 * exp_dev * pair_count // n_exp)
    slots_all = n_exp * cap
    hits = (dest[:, None] == jnp.arange(n_exp, dtype=jnp.int32)[None, :]).astype(jnp.int32)
    before = jnp.cumsum(hits, axis=0) - hits
    rank = jnp.sum(before * hits, axis=1)
    slot = dest * cap + rank
    placement_table = (slot[None, :] == jnp.arange(slots_all, dtype=jnp.int32)[:, None]).astype(
        jnp.bfloat16
    )
    out_ids = jnp.zeros((slots_all,), jnp.int32).at[slot].set(wanted + 1).reshape(n_exp, cap)
    in_ids = lax.all_to_all(out_ids, "exp", split_axis=0, concat_axis=0, tiled=True)
    incoming = in_ids.reshape(-1)
    served_selection = (
        incoming[:, None] - 1 == jnp.arange(exp_dev, dtype=jnp.int32)[None, :]
    ).astype(jnp.bfloat16)
    owners = (incoming[None, :] - 1 == jnp.arange(exp_dev, dtype=jnp.int32)[:, None]).astype(
        jnp.bfloat16
    )
    fwd_rows = shift_mats(row_offs, pixels)
    fwd_cols = shift_mats(col_offs, pixels)
    back_rows = shift_mats(-row_offs, pixels)
    back_cols = shift_mats(-col_offs, pixels)
    intersection = intersection_masks(row_offs, col_offs, pixels).reshape(
        exp_dev, pair_count, 1, pixels, pixels
    )
    kv32 = along_rows.astype(jnp.float32)
    kh32 = along_cols.astype(jnp.float32)
    flat_norm = 1.0 / math.sqrt(2.0 * pair_count * exp_dev * n_exp)
    bkg_parts = []
    terms = None
    for dd in range(det_dev):
        sl = slice(dd, dd + 1)
        image_d = images[:, sl]
        pick_d = pick[:, sl]
        gains = jnp.einsum("edg,gpq->edpq", pick_d, all_flat, precision=high)
        calibrated = (gains * image_d.astype(jnp.float32) - backgrounds[:, sl, None, None]).astype(
            jnp.bfloat16
        )
        half_done = jnp.einsum(
            "edyw,exw->edyx", calibrated, along_cols, preferred_element_type=jnp.float32
        ).astype(jnp.bfloat16)
        matched = jnp.einsum(
            "evy,edyx->edvx", along_rows, half_done, preferred_element_type=jnp.float32
        ).astype(jnp.bfloat16)
        served = jnp.einsum(
            "lm,muqo->luqo", served_selection, matched, preferred_element_type=jnp.float32
        ).astype(jnp.bfloat16)
        served = served.reshape(n_exp, cap * pixels, pixels)
        returned = lax.all_to_all(served, "exp", split_axis=0, concat_axis=0, tiled=True)
        partners = jnp.einsum(
            "fj,fvhm->jvhm",
            placement_table,
            returned.reshape(slots_all, 1, pixels, pixels),
            preferred_element_type=jnp.float32,
        ).astype(jnp.bfloat16)
        moved = apply_shift(partners, fwd_rows, fwd_cols)
        weight = valid_flat[:, sl].astype(jnp.float32).reshape(exp_dev, pair_count, 1, 1, 1)
        moved = moved.reshape(exp_dev, pair_count, 1, pixels, pixels)
        resid = weight * intersection * (matched[:, None].astype(jnp.float32) - moved)
        adj_own = jnp.sum(resid, axis=1)
        resid_low = resid.reshape(queries, 1, pixels, pixels).astype(jnp.bfloat16)
        returned_images = apply_shift(resid_low, back_rows, back_cols).astype(jnp.bfloat16)
        sending_images = jnp.einsum(
            "ea,ajhv->ejhv", placement_table, returned_images, preferred_element_type=jnp.float32
        ).astype(jnp.bfloat16)
        sending_images = sending_images.reshape(n_exp, cap * pixels, pixels)
        arrived = lax.all_to_all(
            sending_images, "exp", split_axis=0, concat_axis=0, tiled=True
        ).reshape(slots_all, 1, pixels, pixels)
        adj_partner = jnp.einsum(
            "js,sdpq->jdpq", owners, arrived, preferred_element_type=jnp.float32
        )
        adj_matched = adj_own - adj_partner
        partial_rows = jnp.einsum("edyx,exw->edyw", adj_matched, kh32, precision=high)
        adj_cal = jnp.einsum("eyv,edyw->edvw", kv32, partial_rows, precision=high)
        bkg_parts.append(-jnp.sum(adj_cal, axis=(2, 3)) / pixels)
        part = jnp.einsum(
            "edg,edpq->gpq", pick_d, image_d.astype(jnp.float32) * adj_cal * flat_norm,
            precision=high,
        )
        terms = part if terms is None else terms + part
    grad_bkg = jnp.concatenate(bkg_parts, axis=1)
    band_rows = pixels // n_exp
    n_det = det_total // det_dev
    by_block = (
        terms.reshape(n_det, det_dev, n_exp, band_rows, pixels)
        .transpose(2, 0, 1, 3, 4)
        .reshape(n_exp * n_det, det_dev, band_rows, pixels)
    )
    grad_flat = jnp.sum(
        lax.all_to_all(by_block, ("exp", "det"), split_axis=0, concat_axis=0, tiled=True),
        axis=0,
    )
    return (grad_flat, grad_bkg)


def solution(mesh):
    return jax.shard_map(
        body,
        mesh=mesh,
        in_specs=(
            P("exp", "det", None, None),
            P("exp", "det"),
            P("det", None, None),
            P("exp", "det"),
            P("exp", None, None),
            P("exp", None),
            P("exp", None),
            P("exp", None, None),
            P("exp", None, "det"),
        ),
        out_specs=(P("det", "exp", None), P("exp", "det")),
        check_vma=False,
    )
```

```python
import math

import jax
import jax.numpy as jnp
from jax import lax
from jax.sharding import PartitionSpec as P


def shift_mats(offs, pixels):
    rows = jnp.arange(pixels, dtype=jnp.int32)
    return (rows[None, None, :] == rows[None, :, None] + offs[:, None, None]).astype(jnp.bfloat16)


def apply_shift(field, row_mats, col_mats):
    partial_cols = jnp.einsum(
        "qduv,qxv->qdux", field, col_mats, preferred_element_type=jnp.float32
    ).astype(jnp.bfloat16)
    return jnp.einsum("qyu,qdux->qdyx", row_mats, partial_cols, preferred_element_type=jnp.float32)


def intersection_masks(row_offs, col_offs, pixels):
    rows = jnp.arange(pixels, dtype=jnp.int32)
    row_in = (rows[None, :] + row_offs[:, None] >= 0) & (rows[None, :] + row_offs[:, None] < pixels)
    col_in = (rows[None, :] + col_offs[:, None] >= 0) & (rows[None, :] + col_offs[:, None] < pixels)
    return (row_in[:, :, None] & col_in[:, None, :]).astype(jnp.float32)


def body(images, det_ids, flat, backgrounds, taps, partner_dev, partner_slot, offsets, pair_valid):
    high = lax.Precision.HIGHEST
    exp_dev, det_dev, pixels = (images.shape[0], images.shape[1], images.shape[2])
    pair_count = partner_dev.shape[1]
    tap_count = taps.shape[2]
    n_exp = lax.axis_size("exp")
    queries = exp_dev * pair_count
    all_flat = lax.all_gather(flat, "det", axis=0, tiled=True)
    det_total = all_flat.shape[0]
    pick = (det_ids[:, :, None] == jnp.arange(det_total, dtype=jnp.int32)[None, None, :]).astype(
        jnp.float32
    )
    rows = jnp.arange(pixels, dtype=jnp.int32)
    lag = rows[None, :] - rows[:, None] + (tap_count - 1) // 2
    table = (lag[:, :, None] == jnp.arange(tap_count, dtype=jnp.int32)[None, None, :]).astype(
        jnp.bfloat16
    )
    bands = jnp.einsum("pqt,ekt->ekpq", table, taps, preferred_element_type=jnp.float32).astype(
        jnp.bfloat16
    )
    along_rows = bands[:, 0]
    along_cols = bands[:, 1]
    dest = partner_dev.reshape(-1)
    wanted = partner_slot.reshape(-1)
    row_offs = offsets[:, :, 0].reshape(-1)
    col_offs = offsets[:, :, 1].reshape(-1)
    valid_flat = pair_valid.reshape(queries, det_dev)
    cap = max(2, 2 * exp_dev * pair_count // n_exp)
    slots_all = n_exp * cap
    hits = (dest[:, None] == jnp.arange(n_exp, dtype=jnp.int32)[None, :]).astype(jnp.int32)
    before = jnp.cumsum(hits, axis=0) - hits
    rank = jnp.sum(before * hits, axis=1)
    slot = dest * cap + rank
    placement_table = (slot[None, :] == jnp.arange(slots_all, dtype=jnp.int32)[:, None]).astype(
        jnp.bfloat16
    )
    out_ids = jnp.zeros((slots_all,), jnp.int32).at[slot].set(wanted + 1).reshape(n_exp, cap)
    in_ids = lax.all_to_all(out_ids, "exp", split_axis=0, concat_axis=0, tiled=True)
    incoming = in_ids.reshape(-1)
    served_selection = (
        incoming[:, None] - 1 == jnp.arange(exp_dev, dtype=jnp.int32)[None, :]
    ).astype(jnp.bfloat16)
    serve_index = jnp.clip(incoming - 1, 0, exp_dev - 1)
    send_index = jnp.zeros((slots_all,), jnp.int32).at[slot].set(
        jnp.arange(queries, dtype=jnp.int32)
    )
    owners = (incoming[None, :] - 1 == jnp.arange(exp_dev, dtype=jnp.int32)[:, None]).astype(
        jnp.bfloat16
    )
    fwd_rows = shift_mats(row_offs, pixels)
    fwd_cols = shift_mats(col_offs, pixels)
    back_rows = shift_mats(-row_offs, pixels)
    back_cols = shift_mats(-col_offs, pixels)
    intersection = intersection_masks(row_offs, col_offs, pixels).reshape(
        exp_dev, pair_count, 1, pixels, pixels
    )
    kv32 = along_rows.astype(jnp.float32)
    kh32 = along_cols.astype(jnp.float32)
    flat_norm = 1.0 / math.sqrt(2.0 * pair_count * exp_dev * n_exp)
    bkg_parts = []
    terms = None
    for dd in range(det_dev):
        sl = slice(dd, dd + 1)
        image_d = images[:, sl]
        pick_d = pick[:, sl]
        gains = jnp.einsum("edg,gpq->edpq", pick_d, all_flat, precision=high)
        calibrated = (gains * image_d.astype(jnp.float32) - backgrounds[:, sl, None, None]).astype(
            jnp.bfloat16
        )
        half_done = jnp.einsum(
            "edyw,exw->edyx", calibrated, along_cols, preferred_element_type=jnp.float32
        ).astype(jnp.bfloat16)
        matched = jnp.einsum(
            "evy,edyx->edvx", along_rows, half_done, preferred_element_type=jnp.float32
        ).astype(jnp.bfloat16)
        served = jnp.take(matched, serve_index, axis=0, mode="clip")
        served = served.reshape(n_exp, cap * pixels, pixels)
        returned = lax.all_to_all(served, "exp", split_axis=0, concat_axis=0, tiled=True)
        partners = jnp.einsum(
            "fj,fvhm->jvhm",
            placement_table,
            returned.reshape(slots_all, 1, pixels, pixels),
            preferred_element_type=jnp.float32,
        ).astype(jnp.bfloat16)
        moved = apply_shift(partners, fwd_rows, fwd_cols)
        weight = valid_flat[:, sl].astype(jnp.float32).reshape(exp_dev, pair_count, 1, 1, 1)
        moved = moved.reshape(exp_dev, pair_count, 1, pixels, pixels)
        resid = weight * intersection * (matched[:, None].astype(jnp.float32) - moved)
        adj_own = jnp.sum(resid, axis=1)
        resid_low = resid.reshape(queries, 1, pixels, pixels).astype(jnp.bfloat16)
        returned_images = apply_shift(resid_low, back_rows, back_cols).astype(jnp.bfloat16)
        sending_images = jnp.take(returned_images, send_index, axis=0, mode="clip")
        sending_images = sending_images.reshape(n_exp, cap * pixels, pixels)
        arrived = lax.all_to_all(
            sending_images, "exp", split_axis=0, concat_axis=0, tiled=True
        ).reshape(slots_all, 1, pixels, pixels)
        adj_partner = jnp.einsum(
            "js,sdpq->jdpq", owners, arrived, preferred_element_type=jnp.float32
        )
        adj_matched = adj_own - adj_partner
        partial_rows = jnp.einsum("edyx,exw->edyw", adj_matched, kh32, precision=high)
        adj_cal = jnp.einsum("eyv,edyw->edvw", kv32, partial_rows, precision=high)
        bkg_parts.append(-jnp.sum(adj_cal, axis=(2, 3)) / pixels)
        part = jnp.einsum(
            "edg,edpq->gpq", pick_d, image_d.astype(jnp.float32) * adj_cal * flat_norm,
            precision=high,
        )
        terms = part if terms is None else terms + part
    grad_bkg = jnp.concatenate(bkg_parts, axis=1)
    band_rows = pixels // n_exp
    n_det = det_total // det_dev
    by_block = (
        terms.reshape(n_det, det_dev, n_exp, band_rows, pixels)
        .transpose(2, 0, 1, 3, 4)
        .reshape(n_exp * n_det, det_dev, band_rows, pixels)
    )
    grad_flat = jnp.sum(
        lax.all_to_all(by_block, ("exp", "det"), split_axis=0, concat_axis=0, tiled=True),
        axis=0,
    )
    return (grad_flat, grad_bkg)


def solution(mesh):
    return jax.shard_map(
        body,
        mesh=mesh,
        in_specs=(
            P("exp", "det", None, None),
            P("exp", "det"),
            P("det", None, None),
            P("exp", "det"),
            P("exp", None, None),
            P("exp", None),
            P("exp", None),
            P("exp", None, None),
            P("exp", None, "det"),
        ),
        out_specs=(P("det", "exp", None), P("exp", "det")),
        check_vma=False,
    )
```

```python
import math

import jax
import jax.numpy as jnp
from jax import lax
from jax.sharding import PartitionSpec as P


def shift_mats(offs, pixels):
    rows = jnp.arange(pixels, dtype=jnp.int32)
    return (rows[None, None, :] == rows[None, :, None] + offs[:, None, None]).astype(jnp.bfloat16)


def apply_shift(field, row_mats, col_mats):
    partial_cols = jnp.einsum(
        "qduv,qxv->qdux", field, col_mats, preferred_element_type=jnp.float32
    ).astype(jnp.bfloat16)
    return jnp.einsum("qyu,qdux->qdyx", row_mats, partial_cols, preferred_element_type=jnp.float32)


def intersection_masks(row_offs, col_offs, pixels):
    rows = jnp.arange(pixels, dtype=jnp.int32)
    row_in = (rows[None, :] + row_offs[:, None] >= 0) & (rows[None, :] + row_offs[:, None] < pixels)
    col_in = (rows[None, :] + col_offs[:, None] >= 0) & (rows[None, :] + col_offs[:, None] < pixels)
    return (row_in[:, :, None] & col_in[:, None, :]).astype(jnp.float32)


def body(images, det_ids, flat, backgrounds, taps, partner_dev, partner_slot, offsets, pair_valid):
    high = lax.Precision.HIGHEST
    exp_dev, det_dev, pixels = (images.shape[0], images.shape[1], images.shape[2])
    pair_count = partner_dev.shape[1]
    tap_count = taps.shape[2]
    n_exp = lax.axis_size("exp")
    queries = exp_dev * pair_count
    det_total = flat.shape[0] * lax.axis_size("det")
    placed = lax.dynamic_update_slice(
        jnp.zeros((det_total,) + flat.shape[1:], flat.dtype),
        flat,
        (lax.axis_index("det") * flat.shape[0], 0, 0),
    )
    all_flat = lax.psum(placed, "det")
    pick = (det_ids[:, :, None] == jnp.arange(det_total, dtype=jnp.int32)[None, None, :]).astype(
        jnp.float32
    )
    rows = jnp.arange(pixels, dtype=jnp.int32)
    lag = rows[None, :] - rows[:, None] + (tap_count - 1) // 2
    table = (lag[:, :, None] == jnp.arange(tap_count, dtype=jnp.int32)[None, None, :]).astype(
        jnp.bfloat16
    )
    bands = jnp.einsum("pqt,ekt->ekpq", table, taps, preferred_element_type=jnp.float32).astype(
        jnp.bfloat16
    )
    along_rows = bands[:, 0]
    along_cols = bands[:, 1]
    dest = partner_dev.reshape(-1)
    wanted = partner_slot.reshape(-1)
    row_offs = offsets[:, :, 0].reshape(-1)
    col_offs = offsets[:, :, 1].reshape(-1)
    valid_flat = pair_valid.reshape(queries, det_dev)
    cap = max(2, 2 * exp_dev * pair_count // n_exp)
    slots_all = n_exp * cap
    hits = (dest[:, None] == jnp.arange(n_exp, dtype=jnp.int32)[None, :]).astype(jnp.int32)
    before = jnp.cumsum(hits, axis=0) - hits
    rank = jnp.sum(before * hits, axis=1)
    slot = dest * cap + rank
    placement_table = (slot[None, :] == jnp.arange(slots_all, dtype=jnp.int32)[:, None]).astype(
        jnp.bfloat16
    )
    out_ids = jnp.zeros((slots_all,), jnp.int32).at[slot].set(wanted + 1).reshape(n_exp, cap)
    in_ids = lax.all_to_all(out_ids, "exp", split_axis=0, concat_axis=0, tiled=True)
    incoming = in_ids.reshape(-1)
    served_selection = (
        incoming[:, None] - 1 == jnp.arange(exp_dev, dtype=jnp.int32)[None, :]
    ).astype(jnp.bfloat16)
    serve_index = jnp.clip(incoming - 1, 0, exp_dev - 1)
    send_index = jnp.zeros((slots_all,), jnp.int32).at[slot].set(
        jnp.arange(queries, dtype=jnp.int32)
    )
    owners = (incoming[None, :] - 1 == jnp.arange(exp_dev, dtype=jnp.int32)[:, None]).astype(
        jnp.bfloat16
    )
    fwd_rows = shift_mats(row_offs, pixels)
    fwd_cols = shift_mats(col_offs, pixels)
    back_rows = shift_mats(-row_offs, pixels)
    back_cols = shift_mats(-col_offs, pixels)
    intersection = intersection_masks(row_offs, col_offs, pixels).reshape(
        exp_dev, pair_count, 1, pixels, pixels
    )
    kv32 = along_rows.astype(jnp.float32)
    kh32 = along_cols.astype(jnp.float32)
    flat_norm = 1.0 / math.sqrt(2.0 * pair_count * exp_dev * n_exp)
    bkg_parts = []
    terms = None
    for dd in range(det_dev):
        sl = slice(dd, dd + 1)
        image_d = images[:, sl]
        pick_d = pick[:, sl]
        gains = jnp.einsum("edg,gpq->edpq", pick_d, all_flat, precision=high)
        calibrated = (gains * image_d.astype(jnp.float32) - backgrounds[:, sl, None, None]).astype(
            jnp.bfloat16
        )
        half_done = jnp.einsum(
            "edyw,exw->edyx", calibrated, along_cols, preferred_element_type=jnp.float32
        ).astype(jnp.bfloat16)
        matched = jnp.einsum(
            "evy,edyx->edvx", along_rows, half_done, preferred_element_type=jnp.float32
        ).astype(jnp.bfloat16)
        served = jnp.take(matched, serve_index, axis=0, mode="clip")
        served = served.reshape(n_exp, cap * pixels, pixels)
        returned = lax.all_to_all(served, "exp", split_axis=0, concat_axis=0, tiled=True)
        partners = jnp.einsum(
            "fj,fvhm->jvhm",
            placement_table,
            returned.reshape(slots_all, 1, pixels, pixels),
            preferred_element_type=jnp.float32,
        ).astype(jnp.bfloat16)
        moved = apply_shift(partners, fwd_rows, fwd_cols)
        weight = valid_flat[:, sl].astype(jnp.float32).reshape(exp_dev, pair_count, 1, 1, 1)
        moved = moved.reshape(exp_dev, pair_count, 1, pixels, pixels)
        resid = weight * intersection * (matched[:, None].astype(jnp.float32) - moved)
        adj_own = jnp.sum(resid, axis=1)
        resid_low = resid.reshape(queries, 1, pixels, pixels).astype(jnp.bfloat16)
        returned_images = apply_shift(resid_low, back_rows, back_cols).astype(jnp.bfloat16)
        sending_images = jnp.take(returned_images, send_index, axis=0, mode="clip")
        sending_images = sending_images.reshape(n_exp, cap * pixels, pixels)
        arrived = lax.all_to_all(
            sending_images, "exp", split_axis=0, concat_axis=0, tiled=True
        ).reshape(slots_all, 1, pixels, pixels)
        adj_partner = jnp.einsum(
            "js,sdpq->jdpq", owners, arrived, preferred_element_type=jnp.float32
        )
        adj_matched = adj_own - adj_partner
        partial_rows = jnp.einsum("edyx,exw->edyw", adj_matched, kh32, precision=high)
        adj_cal = jnp.einsum("eyv,edyw->edvw", kv32, partial_rows, precision=high)
        bkg_parts.append(-jnp.sum(adj_cal, axis=(2, 3)) / pixels)
        part = jnp.einsum(
            "edg,edpq->gpq", pick_d, image_d.astype(jnp.float32) * adj_cal * flat_norm,
            precision=high,
        )
        terms = part if terms is None else terms + part
    grad_bkg = jnp.concatenate(bkg_parts, axis=1)
    band_rows = pixels // n_exp
    n_det = det_total // det_dev
    by_block = (
        terms.reshape(n_det, det_dev, n_exp, band_rows, pixels)
        .transpose(2, 0, 1, 3, 4)
        .reshape(n_exp * n_det, det_dev, band_rows, pixels)
    )
    grad_flat = jnp.sum(
        lax.all_to_all(by_block, ("exp", "det"), split_axis=0, concat_axis=0, tiled=True),
        axis=0,
    )
    return (grad_flat, grad_bkg)


def solution(mesh):
    return jax.shard_map(
        body,
        mesh=mesh,
        in_specs=(
            P("exp", "det", None, None),
            P("exp", "det"),
            P("det", None, None),
            P("exp", "det"),
            P("exp", None, None),
            P("exp", None),
            P("exp", None),
            P("exp", None, None),
            P("exp", None, "det"),
        ),
        out_specs=(P("det", "exp", None), P("exp", "det")),
        check_vma=False,
    )
```
